32 devices in a mesh: groups: 2 (over x), rows: 16 (over z, y, core).
Axes of the slice: x: 2, y: 2, z: 4, core: 2. Of those that a mesh axis runs over, the one named last changes fastest.
Arguments:
- student: float32 [8192, 512], P(('groups', 'rows')), parts along dimension 0, may hold values from -6 to 6
- teacher: float32 [8192, 6144], P(('groups', 'rows')), parts along dimension 0, may hold values from -6 to 6
- heads: bfloat16 [512, 6144], P(None, 'rows'), may hold values from -0.25 to 0.25
Outputs:
- grad_student: float32 [8192, 512], P(('groups', 'rows')), parts along dimension 0
- grad_heads: float32 [1024, 6144], P('groups', 'rows'), parts along dimension 0
The draws below stay inside these ranges and needn't reach their ends.
There are 2 independent parts, one for each index of `groups`. The reference program is written for one: setup_inputs(seed, part) draws one part's arguments, and reference() takes and returns one part's arrays. A program takes and returns all parts, laid end to end along the dimension named above; an argument that names none is the same for every part. Nothing has to cross between parts.
All inputs are finite; a program needn't handle non-finite values.
Results may differ from the reference program's by a relative error of at most 0.0026.
Values may be sent and summed in bfloat16 or wider, within the bound.
No kernel may reach another device: no remote copies, remote signals or barrier semaphores. Data moves between devices by JAX's collectives and lax.ppermute only.
A program may use at most 128 MiB of HBM per device.

```python
import jax
import jax.numpy as jnp
from jax import lax

D = 512
F = 6144
ROWS = 4096


def block_scale(own_key, dims, pieces, smallest, high):
    loudness, own = 1.0, jax.random.fold_in(own_key, 6)
    for position, shards_of in pieces:
        draws = jnp.exp(jax.random.uniform(jax.random.fold_in(own, position), (shards_of,), jnp.float32, smallest / len(pieces), high / len(pieces)))
        loudness = loudness * jnp.repeat(draws, dims[position] // shards_of).reshape([-1 if axis == position else 1 for axis in range(len(dims))])
    return loudness


def bell_draw(own_key, shape, deviation, reach, pieces=(), dtype=jnp.bfloat16):
    values = jax.random.normal(own_key, shape, jnp.float32) * deviation
    if len(pieces) > 0:
        values = block_scale(own_key, shape, pieces, -0.22, 0.18) * values
    return jnp.clip(values, min=-reach, max=reach).astype(dtype)


def setup_inputs(seed: int = 0, part: int = 0) -> dict:
    splits = jax.random.split(jax.random.key(seed), 4)
    part_keys = jax.random.split(jax.random.fold_in(splits[3], part), 4)
    student = bell_draw(part_keys[0], (ROWS, D), 1.0, 6.0, ((0, 16),), jnp.float32)
    teacher = bell_draw(part_keys[1], (ROWS, F), 1.0, 6.0, ((0, 16),), jnp.float32)
    heads = bell_draw(splits[2], (D, F), D ** -0.5, 0.25, ((1, 16),))
    return {"student": student, "teacher": teacher, "heads": heads}


reg_weight = 0.0625
head_scale = 0.015625


def contract(left, right, left_dim, right_dim):
    return lax.dot_general(left, right, (((left_dim,), (right_dim,)), ((), ())), precision=lax.Precision.HIGHEST, preferred_element_type=jnp.float32)


def reference(student, teacher, heads):
    wide = heads.astype(jnp.float32)
    error = contract(student, wide, 1, 0) - teacher
    cross = contract(teacher, student, 0, 0)
    cross_low = lax.optimization_barrier(cross.astype(jnp.bfloat16)).astype(jnp.float32)
    moment = contract(student, student, 0, 0)
    positions = jnp.arange(D)
    weights = 1.0 + (positions < D // 4).astype(jnp.float32) + (positions < D // 2).astype(jnp.float32)
    nested = jnp.minimum(weights[:, None], weights[None, :])
    gram_scale = 0.5 / ROWS
    grad_student = reg_weight * contract(error, wide, 1, 1) + gram_scale * (contract(student, moment * nested, 1, 0) - contract(teacher, cross_low, 1, 0) * weights[None, :])
    grad_heads = head_scale * (contract(moment, wide, 1, 0) - cross.T)
    return grad_student, grad_heads
```

```python
import jax
import jax.numpy as jnp
from jax import lax
from jax.sharding import PartitionSpec as P

reg_weight = 0.0625
head_scale = 0.015625


def contract(left, right, left_dim, right_dim, precision=lax.Precision.HIGHEST):
    return lax.dot_general(
        left,
        right,
        (((left_dim,), (right_dim,)), ((), ())),
        precision=precision,
        preferred_element_type=jnp.float32,
    )


def split_bf16(x):
    high = x.astype(jnp.bfloat16)
    low = (x - high.astype(jnp.float32)).astype(jnp.bfloat16)
    return high, low


def per_device(student, teacher, heads):
    devices = lax.axis_size("rows")
    rows_here, model_width = student.shape
    teacher_width = teacher.shape[1]
    total_rows = rows_here * devices
    f_here = teacher_width // devices
    d_here = model_width // devices
    positions = jnp.arange(model_width)
    weights = (
        1.0
        + (positions < model_width // 4).astype(jnp.float32)
        + (positions < model_width // 2).astype(jnp.float32)
    )
    nested = jnp.minimum(weights[:, None], weights[None, :])
    gram_scale = 0.5 / total_rows

    heads_all = lax.all_gather(heads, "rows", axis=1, tiled=True)

    left = jnp.concatenate(
        [
            teacher.reshape(rows_here, devices, f_here),
            student.reshape(rows_here, devices, d_here),
        ],
        axis=2,
    ).reshape(rows_here, devices * (f_here + d_here))
    partial = contract(left, student, 0, 0, lax.Precision.HIGH)
    reduced = lax.psum_scatter(partial, "rows", scatter_dimension=0, tiled=True)
    cross_here = reduced[:f_here]
    moment_here = reduced[f_here:]

    moment_high, moment_low = split_bf16(moment_here)
    packed = jnp.concatenate(
        [cross_here.astype(jnp.bfloat16), moment_high, moment_low], axis=0
    )
    gathered = lax.all_gather(packed, "rows", axis=0, tiled=False)
    cross_low = gathered[:, :f_here].reshape(teacher_width, model_width)
    moment = (
        gathered[:, f_here : f_here + d_here].astype(jnp.float32)
        + gathered[:, f_here + d_here :].astype(jnp.float32)
    ).reshape(model_width, model_width)

    grad_heads = head_scale * (
        contract(moment, heads.astype(jnp.float32), 1, 0) - cross_here.T
    )

    gram_heads = contract(heads_all, heads_all, 1, 1, lax.Precision.DEFAULT)
    teacher_high, teacher_low = split_bf16(teacher)
    teacher_heads = contract(teacher_high, heads_all, 1, 1, lax.Precision.DEFAULT) + contract(
        teacher_low, heads_all, 1, 1, lax.Precision.DEFAULT
    )
    teacher_cross = contract(teacher_high, cross_low, 1, 0, lax.Precision.DEFAULT) + contract(
        teacher_low, cross_low, 1, 0, lax.Precision.DEFAULT
    )
    student_side = reg_weight * gram_heads + gram_scale * (moment * nested)
    grad_student = (
        contract(student, student_side, 1, 0)
        - reg_weight * teacher_heads
        - gram_scale * teacher_cross * weights[None, :]
    )
    return (grad_student, grad_heads)


def solution(mesh):
    in_specs = (P(("groups", "rows"), None), P(("groups", "rows"), None), P(None, "rows"))
    out_specs = (P(("groups", "rows"), None), P("groups", "rows"))
    return jax.shard_map(
        per_device, mesh=mesh, in_specs=in_specs, out_specs=out_specs, check_vma=False
    )
```

```python
import jax
import jax.numpy as jnp
from jax import lax
from jax.sharding import PartitionSpec as P

reg_weight = 0.0625
head_scale = 0.015625


def contract(left, right, left_dim, right_dim, precision=lax.Precision.HIGHEST):
    return lax.dot_general(
        left,
        right,
        (((left_dim,), (right_dim,)), ((), ())),
        precision=precision,
        preferred_element_type=jnp.float32,
    )


def split_bf16(x):
    high = lax.reduce_precision(x, exponent_bits=8, mantissa_bits=7)
    low = (x - high).astype(jnp.bfloat16)
    return high.astype(jnp.bfloat16), low


def bit_reverse_table(n):
    bits = n.bit_length() - 1
    return [int(format(j, "0%db" % bits)[::-1], 2) if bits else 0 for j in range(n)]


def gather_by_doubling(block, axis_name, axis):
    n = lax.axis_size(axis_name)
    me = lax.axis_index(axis_name)
    held = block
    bit = n.bit_length() - 2
    while bit >= 0:
        step = 1 << bit
        pairs = [(i, i ^ step) for i in range(n)]
        held = jnp.concatenate([held, lax.ppermute(held, axis_name, pairs)], axis=axis)
        bit -= 1
    rev = jnp.array(bit_reverse_table(n), jnp.int32)
    order = rev[me] ^ rev
    shape = held.shape
    blocks = held.reshape(shape[:axis] + (n, shape[axis] // n) + shape[axis + 1 :])
    blocks = jnp.take(blocks, order, axis=axis)
    return blocks.reshape(shape)


def per_device(student, teacher, heads):
    devices = lax.axis_size("rows")
    rows_here, model_width = student.shape
    teacher_width = teacher.shape[1]
    total_rows = rows_here * devices
    f_here = teacher_width // devices
    d_here = model_width // devices
    positions = jnp.arange(model_width)
    weights = (
        1.0
        + (positions < model_width // 4).astype(jnp.float32)
        + (positions < model_width // 2).astype(jnp.float32)
    )
    nested = jnp.minimum(weights[:, None], weights[None, :])
    gram_scale = 0.5 / total_rows

    heads_all = gather_by_doubling(heads, "rows", 1)

    left = jnp.concatenate(
        [
            teacher.reshape(rows_here, devices, f_here),
            student.reshape(rows_here, devices, d_here),
        ],
        axis=2,
    ).reshape(rows_here, devices * (f_here + d_here))
    partial = contract(left, student, 0, 0, lax.Precision.HIGH)
    reduced = lax.psum_scatter(partial, "rows", scatter_dimension=0, tiled=True)
    cross_here = reduced[:f_here]
    moment_here = reduced[f_here:]

    moment_high, moment_low = split_bf16(moment_here)
    packed = jnp.concatenate(
        [cross_here.astype(jnp.bfloat16), moment_high, moment_low], axis=0
    )
    gathered = lax.all_gather(packed, "rows", axis=0, tiled=False)
    cross_low = gathered[:, :f_here].reshape(teacher_width, model_width)
    moment = (
        gathered[:, f_here : f_here + d_here].astype(jnp.float32)
        + gathered[:, f_here + d_here :].astype(jnp.float32)
    ).reshape(model_width, model_width)

    grad_heads = head_scale * (
        contract(moment, heads.astype(jnp.float32), 1, 0) - cross_here.T
    )

    gram_heads = contract(heads_all, heads_all, 1, 1, lax.Precision.DEFAULT)
    teacher_high, teacher_low = split_bf16(teacher)
    teacher_heads = contract(teacher_high, heads_all, 1, 1, lax.Precision.DEFAULT) + contract(
        teacher_low, heads_all, 1, 1, lax.Precision.DEFAULT
    )
    teacher_cross = contract(teacher_high, cross_low, 1, 0, lax.Precision.DEFAULT) + contract(
        teacher_low, cross_low, 1, 0, lax.Precision.DEFAULT
    )
    student_side = reg_weight * gram_heads + gram_scale * (moment * nested)
    grad_student = (
        contract(student, student_side, 1, 0)
        - reg_weight * teacher_heads
        - gram_scale * teacher_cross * weights[None, :]
    )
    return (grad_student, grad_heads)


def solution(mesh):
    in_specs = (P(("groups", "rows"), None), P(("groups", "rows"), None), P(None, "rows"))
    out_specs = (P(("groups", "rows"), None), P("groups", "rows"))
    return jax.shard_map(
        per_device, mesh=mesh, in_specs=in_specs, out_specs=out_specs, check_vma=False
    )
```

```python
import jax
import jax.numpy as jnp
from jax import lax
from jax.sharding import PartitionSpec as P

reg_weight = 0.0625
head_scale = 0.015625


def contract(left, right, left_dim, right_dim, precision=lax.Precision.HIGHEST):
    return lax.dot_general(
        left,
        right,
        (((left_dim,), (right_dim,)), ((), ())),
        precision=precision,
        preferred_element_type=jnp.float32,
    )


def split_bf16(x):
    high = lax.reduce_precision(x, exponent_bits=8, mantissa_bits=7)
    low = (x - high).astype(jnp.bfloat16)
    return high.astype(jnp.bfloat16), low


def bit_reverse_table(n):
    bits = n.bit_length() - 1
    return [int(format(j, "0%db" % bits)[::-1], 2) if bits else 0 for j in range(n)]


def gather_by_doubling(block, axis_name, axis):
    n = lax.axis_size(axis_name)
    me = lax.axis_index(axis_name)
    held = block
    bit = n.bit_length() - 2
    while bit >= 0:
        step = 1 << bit
        pairs = [(i, i ^ step) for i in range(n)]
        held = jnp.concatenate([held, lax.ppermute(held, axis_name, pairs)], axis=axis)
        bit -= 1
    rev = jnp.array(bit_reverse_table(n), jnp.int32)
    order = rev[me] ^ rev
    shape = held.shape
    blocks = held.reshape(shape[:axis] + (n, shape[axis] // n) + shape[axis + 1 :])
    blocks = jnp.take(blocks, order, axis=axis)
    return blocks.reshape(shape)


def per_device(student, teacher, heads):
    devices = lax.axis_size("rows")
    rows_here, model_width = student.shape
    teacher_width = teacher.shape[1]
    total_rows = rows_here * devices
    f_here = teacher_width // devices
    d_here = model_width // devices
    positions = jnp.arange(model_width)
    weights = (
        1.0
        + (positions < model_width // 4).astype(jnp.float32)
        + (positions < model_width // 2).astype(jnp.float32)
    )
    nested = jnp.minimum(weights[:, None], weights[None, :])
    gram_scale = 0.5 / total_rows

    heads_all = lax.all_gather(heads, "rows", axis=1, tiled=True)

    left = jnp.concatenate(
        [
            teacher.reshape(rows_here, devices, f_here),
            student.reshape(rows_here, devices, d_here),
        ],
        axis=2,
    ).reshape(rows_here, devices * (f_here + d_here))
    partial = contract(left, student, 0, 0, lax.Precision.HIGH)
    heads_all, partial = lax.optimization_barrier((heads_all, partial))
    reduced = lax.psum_scatter(partial, "rows", scatter_dimension=0, tiled=True)
    cross_here = reduced[:f_here]
    moment_here = reduced[f_here:]

    moment_high, moment_low = split_bf16(moment_here)
    packed = jnp.concatenate(
        [cross_here.astype(jnp.bfloat16), moment_high, moment_low], axis=0
    )
    gathered = lax.all_gather(packed, "rows", axis=0, tiled=False)
    cross_low = gathered[:, :f_here].reshape(teacher_width, model_width)
    moment = (
        gathered[:, f_here : f_here + d_here].astype(jnp.float32)
        + gathered[:, f_here + d_here :].astype(jnp.float32)
    ).reshape(model_width, model_width)

    grad_heads = head_scale * (
        contract(moment, heads.astype(jnp.float32), 1, 0) - cross_here.T
    )

    gram_heads = contract(heads_all, heads_all, 1, 1, lax.Precision.DEFAULT)
    teacher_high, teacher_low = split_bf16(teacher)
    teacher_heads = contract(teacher_high, heads_all, 1, 1, lax.Precision.DEFAULT) + contract(
        teacher_low, heads_all, 1, 1, lax.Precision.DEFAULT
    )
    teacher_cross = contract(teacher_high, cross_low, 1, 0, lax.Precision.DEFAULT) + contract(
        teacher_low, cross_low, 1, 0, lax.Precision.DEFAULT
    )
    student_side = reg_weight * gram_heads + gram_scale * (moment * nested)
    grad_student = (
        contract(student, student_side, 1, 0)
        - reg_weight * teacher_heads
        - gram_scale * teacher_cross * weights[None, :]
    )
    return (grad_student, grad_heads)


def solution(mesh):
    in_specs = (P(("groups", "rows"), None), P(("groups", "rows"), None), P(None, "rows"))
    out_specs = (P(("groups", "rows"), None), P("groups", "rows"))
    return jax.shard_map(
        per_device, mesh=mesh, in_specs=in_specs, out_specs=out_specs, check_vma=False
    )
```

```python
import jax
import jax.numpy as jnp
from jax import lax
from jax.sharding import PartitionSpec as P

reg_weight = 0.0625
head_scale = 0.015625


def contract(left, right, left_dim, right_dim, precision=lax.Precision.HIGHEST):
    return lax.dot_general(
        left,
        right,
        (((left_dim,), (right_dim,)), ((), ())),
        precision=precision,
        preferred_element_type=jnp.float32,
    )


def split_bf16(x):
    high = lax.reduce_precision(x, exponent_bits=8, mantissa_bits=7)
    low = (x - high).astype(jnp.bfloat16)
    return high.astype(jnp.bfloat16), low


def bit_reverse_table(n):
    bits = n.bit_length() - 1
    return [int(format(j, "0%db" % bits)[::-1], 2) if bits else 0 for j in range(n)]


def gather_by_doubling(block, axis_name, axis):
    n = lax.axis_size(axis_name)
    me = lax.axis_index(axis_name)
    held = block
    bit = n.bit_length() - 2
    while bit >= 0:
        step = 1 << bit
        pairs = [(i, i ^ step) for i in range(n)]
        held = jnp.concatenate([held, lax.ppermute(held, axis_name, pairs)], axis=axis)
        bit -= 1
    rev = jnp.array(bit_reverse_table(n), jnp.int32)
    order = rev[me] ^ rev
    shape = held.shape
    blocks = held.reshape(shape[:axis] + (n, shape[axis] // n) + shape[axis + 1 :])
    blocks = jnp.take(blocks, order, axis=axis)
    return blocks.reshape(shape)


def per_device(student, teacher, heads):
    chips = lax.axis_size("chips")
    cores = lax.axis_size("core")
    devices = chips * cores
    rows_here, model_width = student.shape
    teacher_width = teacher.shape[1]
    total_rows = rows_here * devices
    f_here = teacher_width // devices
    d_here = model_width // devices
    positions = jnp.arange(model_width)
    weights = (
        1.0
        + (positions < model_width // 4).astype(jnp.float32)
        + (positions < model_width // 2).astype(jnp.float32)
    )
    nested = jnp.minimum(weights[:, None], weights[None, :])
    gram_scale = 0.5 / total_rows

    def core_major(x, width):
        return x.reshape(rows_here, chips, cores, width).transpose(0, 2, 1, 3)

    teacher_cm = core_major(teacher, f_here)

    heads_chips = lax.all_gather(heads, "chips", axis=0, tiled=False)
    heads_all = lax.all_gather(heads_chips, "core", axis=0, tiled=False)
    heads_all = heads_all.transpose(2, 0, 1, 3).reshape(model_width, teacher_width)

    left = jnp.concatenate(
        [teacher_cm, core_major(student, d_here)], axis=3
    ).reshape(rows_here, devices * (f_here + d_here))
    partial = contract(left, student, 0, 0, lax.Precision.HIGH)
    heads_all, partial = lax.optimization_barrier((heads_all, partial))
    reduced = lax.psum_scatter(partial, "core", scatter_dimension=0, tiled=True)
    reduced = lax.psum_scatter(reduced, "chips", scatter_dimension=0, tiled=True)
    cross_here = reduced[:f_here]
    moment_here = reduced[f_here:]

    moment_high, moment_low = split_bf16(moment_here)
    packed = jnp.concatenate(
        [cross_here.astype(jnp.bfloat16), moment_high, moment_low], axis=0
    )
    gathered = lax.all_gather(packed, "chips", axis=0, tiled=False)
    gathered = lax.all_gather(gathered, "core", axis=0, tiled=False)
    cross_low = gathered[:, :, :f_here].reshape(teacher_width, model_width)
    moment = (
        gathered[:, :, f_here : f_here + d_here].astype(jnp.float32)
        + gathered[:, :, f_here + d_here :].astype(jnp.float32)
    )
    moment = moment.transpose(1, 0, 2, 3).reshape(model_width, model_width)

    grad_heads = head_scale * (
        contract(moment, heads.astype(jnp.float32), 1, 0) - cross_here.T
    )

    gram_heads = contract(heads_all, heads_all, 1, 1, lax.Precision.DEFAULT)
    teacher_high, teacher_low = split_bf16(teacher_cm.reshape(rows_here, teacher_width))
    teacher_heads = contract(teacher_high, heads_all, 1, 1, lax.Precision.DEFAULT) + contract(
        teacher_low, heads_all, 1, 1, lax.Precision.DEFAULT
    )
    teacher_cross = contract(teacher_high, cross_low, 1, 0, lax.Precision.DEFAULT) + contract(
        teacher_low, cross_low, 1, 0, lax.Precision.DEFAULT
    )
    student_side = reg_weight * gram_heads + gram_scale * (moment * nested)
    grad_student = (
        contract(student, student_side, 1, 0)
        - reg_weight * teacher_heads
        - gram_scale * teacher_cross * weights[None, :]
    )
    return (grad_student, grad_heads)


def solution(mesh):
    groups, devices = mesh.devices.shape
    cores = 2 if devices % 2 == 0 else 1
    chip_mesh = jax.sharding.Mesh(
        mesh.devices.reshape(groups, devices // cores, cores), ("groups", "chips", "core")
    )
    rows = ("groups", "chips", "core")
    in_specs = (P(rows, None), P(rows, None), P(None, ("chips", "core")))
    out_specs = (P(rows, None), P("groups", ("chips", "core")))
    return jax.shard_map(
        per_device, mesh=chip_mesh, in_specs=in_specs, out_specs=out_specs, check_vma=False
    )
```

```python
import jax
import jax.numpy as jnp
from jax import lax
from jax.sharding import PartitionSpec as P

reg_weight = 0.0625
head_scale = 0.015625


def contract(left, right, left_dim, right_dim, precision=lax.Precision.HIGHEST):
    return lax.dot_general(
        left,
        right,
        (((left_dim,), (right_dim,)), ((), ())),
        precision=precision,
        preferred_element_type=jnp.float32,
    )


def split_bf16(x):
    high = lax.reduce_precision(x, exponent_bits=8, mantissa_bits=7)
    low = (x - high).astype(jnp.bfloat16)
    return high.astype(jnp.bfloat16), low


def bit_reverse_table(n):
    bits = n.bit_length() - 1
    return [int(format(j, "0%db" % bits)[::-1], 2) if bits else 0 for j in range(n)]


def gather_by_doubling(block, axis_name, axis):
    n = lax.axis_size(axis_name)
    me = lax.axis_index(axis_name)
    held = block
    bit = n.bit_length() - 2
    while bit >= 0:
        step = 1 << bit
        pairs = [(i, i ^ step) for i in range(n)]
        held = jnp.concatenate([held, lax.ppermute(held, axis_name, pairs)], axis=axis)
        bit -= 1
    rev = jnp.array(bit_reverse_table(n), jnp.int32)
    order = rev[me] ^ rev
    shape = held.shape
    blocks = held.reshape(shape[:axis] + (n, shape[axis] // n) + shape[axis + 1 :])
    blocks = jnp.take(blocks, order, axis=axis)
    return blocks.reshape(shape)


def per_device(student, teacher, heads):
    devices = lax.axis_size("rows")
    rows_here, model_width = student.shape
    teacher_width = teacher.shape[1]
    total_rows = rows_here * devices
    f_here = teacher_width // devices
    d_here = model_width // devices
    positions = jnp.arange(model_width)
    weights = (
        1.0
        + (positions < model_width // 4).astype(jnp.float32)
        + (positions < model_width // 2).astype(jnp.float32)
    )
    nested = jnp.minimum(weights[:, None], weights[None, :])
    gram_scale = 0.5 / total_rows

    group = lax.axis_index("groups")
    half = heads.shape[1] // 2
    mine = lax.dynamic_slice_in_dim(heads, group * half, half, axis=1)
    mine = lax.all_gather(mine, "rows", axis=0, tiled=False)

    left = jnp.concatenate(
        [
            teacher.reshape(rows_here, devices, f_here),
            student.reshape(rows_here, devices, d_here),
        ],
        axis=2,
    ).reshape(rows_here, devices * (f_here + d_here))
    partial = contract(left, student, 0, 0, lax.Precision.HIGH)
    mine, partial = lax.optimization_barrier((mine, partial))
    theirs = lax.ppermute(mine, "groups", [(0, 1), (1, 0)])
    first = group == 0
    heads_all = jnp.stack(
        [jnp.where(first, mine, theirs), jnp.where(first, theirs, mine)], axis=1
    )
    heads_all = heads_all.transpose(2, 0, 1, 3).reshape(model_width, teacher_width)
    reduced = lax.psum_scatter(partial, "rows", scatter_dimension=0, tiled=True)
    cross_here = reduced[:f_here]
    moment_here = reduced[f_here:]

    moment_high, moment_low = split_bf16(moment_here)
    packed = jnp.concatenate(
        [cross_here.astype(jnp.bfloat16), moment_high, moment_low], axis=0
    )
    gathered = lax.all_gather(packed, "rows", axis=0, tiled=False)
    cross_low = gathered[:, :f_here].reshape(teacher_width, model_width)
    moment = (
        gathered[:, f_here : f_here + d_here].astype(jnp.float32)
        + gathered[:, f_here + d_here :].astype(jnp.float32)
    ).reshape(model_width, model_width)

    grad_heads = head_scale * (
        contract(moment, heads.astype(jnp.float32), 1, 0) - cross_here.T
    )

    gram_heads = contract(heads_all, heads_all, 1, 1, lax.Precision.DEFAULT)
    teacher_high, teacher_low = split_bf16(teacher)
    teacher_heads = contract(teacher_high, heads_all, 1, 1, lax.Precision.DEFAULT) + contract(
        teacher_low, heads_all, 1, 1, lax.Precision.DEFAULT
    )
    teacher_cross = contract(teacher_high, cross_low, 1, 0, lax.Precision.DEFAULT) + contract(
        teacher_low, cross_low, 1, 0, lax.Precision.DEFAULT
    )
    student_side = reg_weight * gram_heads + gram_scale * (moment * nested)
    grad_student = (
        contract(student, student_side, 1, 0)
        - reg_weight * teacher_heads
        - gram_scale * teacher_cross * weights[None, :]
    )
    return (grad_student, grad_heads)


def solution(mesh):
    in_specs = (P(("groups", "rows"), None), P(("groups", "rows"), None), P(None, "rows"))
    out_specs = (P(("groups", "rows"), None), P("groups", "rows"))
    return jax.shard_map(
        per_device, mesh=mesh, in_specs=in_specs, out_specs=out_specs, check_vma=False
    )
```

```python
import jax
import jax.numpy as jnp
from jax import lax
from jax.sharding import PartitionSpec as P

reg_weight = 0.0625
head_scale = 0.015625


def contract(left, right, left_dim, right_dim, precision=lax.Precision.HIGHEST):
    return lax.dot_general(
        left,
        right,
        (((left_dim,), (right_dim,)), ((), ())),
        precision=precision,
        preferred_element_type=jnp.float32,
    )


def split_bf16(x):
    high = lax.reduce_precision(x, exponent_bits=8, mantissa_bits=7)
    low = (x - high).astype(jnp.bfloat16)
    return high.astype(jnp.bfloat16), low


def bit_reverse_table(n):
    bits = n.bit_length() - 1
    return [int(format(j, "0%db" % bits)[::-1], 2) if bits else 0 for j in range(n)]


def gather_by_doubling(block, axis_name, axis):
    n = lax.axis_size(axis_name)
    me = lax.axis_index(axis_name)
    held = block
    bit = n.bit_length() - 2
    while bit >= 0:
        step = 1 << bit
        pairs = [(i, i ^ step) for i in range(n)]
        held = jnp.concatenate([held, lax.ppermute(held, axis_name, pairs)], axis=axis)
        bit -= 1
    rev = jnp.array(bit_reverse_table(n), jnp.int32)
    order = rev[me] ^ rev
    shape = held.shape
    blocks = held.reshape(shape[:axis] + (n, shape[axis] // n) + shape[axis + 1 :])
    blocks = jnp.take(blocks, order, axis=axis)
    return blocks.reshape(shape)


def per_device(student, teacher, heads):
    devices = lax.axis_size("rows")
    rows_here, model_width = student.shape
    teacher_width = teacher.shape[1]
    total_rows = rows_here * devices
    f_here = teacher_width // devices
    positions = jnp.arange(model_width)
    weights = (
        1.0
        + (positions < model_width // 4).astype(jnp.float32)
        + (positions < model_width // 2).astype(jnp.float32)
    )
    nested = jnp.minimum(weights[:, None], weights[None, :])
    gram_scale = 0.5 / total_rows

    cross_part = contract(teacher, student, 0, 0, lax.Precision.HIGH)
    moment_part = contract(student, student, 0, 0)
    d_here = model_width // devices
    partial = jnp.concatenate(
        [
            cross_part.reshape(devices, f_here, model_width),
            moment_part.reshape(devices, d_here, model_width),
        ],
        axis=1,
    ).reshape(devices * (f_here + d_here), model_width)
    reduced = lax.psum_scatter(partial, "rows", scatter_dimension=0, tiled=True)
    cross_here = reduced[:f_here]
    moment_here = reduced[f_here:]

    moment_high, moment_low = split_bf16(moment_here)
    pair = jnp.concatenate([moment_high, moment_low], axis=1).reshape(-1)
    spare = -(-pair.shape[0] // (f_here * 128)) * 128
    pair = jnp.pad(pair, (0, f_here * spare - pair.shape[0])).reshape(f_here, spare)
    wide_here = jnp.concatenate([cross_here.astype(jnp.bfloat16), heads.T, pair], axis=1)
    wide_all = lax.all_gather(wide_here, "rows", axis=0, tiled=True)
    moment_all = wide_all[:, 2 * model_width :].reshape(devices, f_here * spare)
    moment_all = moment_all[:, : 2 * d_here * model_width].reshape(
        devices, d_here, 2 * model_width
    )
    moment = (
        moment_all[:, :, :model_width].astype(jnp.float32)
        + moment_all[:, :, model_width:].astype(jnp.float32)
    ).reshape(model_width, model_width)
    heads_all = wide_all[:, model_width : 2 * model_width]

    grad_heads = head_scale * (
        contract(moment, heads.astype(jnp.float32), 1, 0) - cross_here.T
    )

    gram_heads = contract(heads_all, heads_all, 0, 0, lax.Precision.DEFAULT)
    teacher_high, teacher_low = split_bf16(teacher)
    teacher_wide = contract(teacher_high, wide_all, 1, 0, lax.Precision.DEFAULT) + contract(
        teacher_low, wide_all, 1, 0, lax.Precision.DEFAULT
    )
    teacher_cross = teacher_wide[:, :model_width]
    teacher_heads = teacher_wide[:, model_width : 2 * model_width]
    student_side = reg_weight * gram_heads + gram_scale * (moment * nested)
    grad_student = (
        contract(student, student_side, 1, 0)
        - reg_weight * teacher_heads
        - gram_scale * teacher_cross * weights[None, :]
    )
    return (grad_student, grad_heads)


def solution(mesh):
    in_specs = (P(("groups", "rows"), None), P(("groups", "rows"), None), P(None, "rows"))
    out_specs = (P(("groups", "rows"), None), P("groups", "rows"))
    return jax.shard_map(
        per_device, mesh=mesh, in_specs=in_specs, out_specs=out_specs, check_vma=False
    )
```

```python
import jax
import jax.numpy as jnp
from jax import lax
from jax.sharding import PartitionSpec as P

reg_weight = 0.0625
head_scale = 0.015625


def contract(left, right, left_dim, right_dim, precision=lax.Precision.HIGHEST):
    return lax.dot_general(
        left,
        right,
        (((left_dim,), (right_dim,)), ((), ())),
        precision=precision,
        preferred_element_type=jnp.float32,
    )


def split_bf16(x):
    high = lax.reduce_precision(x, exponent_bits=8, mantissa_bits=7)
    low = (x - high).astype(jnp.bfloat16)
    return high.astype(jnp.bfloat16), low


def bit_reverse_table(n):
    bits = n.bit_length() - 1
    return [int(format(j, "0%db" % bits)[::-1], 2) if bits else 0 for j in range(n)]


def gather_by_doubling(block, axis_name, axis):
    n = lax.axis_size(axis_name)
    me = lax.axis_index(axis_name)
    held = block
    bit = n.bit_length() - 2
    while bit >= 0:
        step = 1 << bit
        pairs = [(i, i ^ step) for i in range(n)]
        held = jnp.concatenate([held, lax.ppermute(held, axis_name, pairs)], axis=axis)
        bit -= 1
    rev = jnp.array(bit_reverse_table(n), jnp.int32)
    order = rev[me] ^ rev
    shape = held.shape
    blocks = held.reshape(shape[:axis] + (n, shape[axis] // n) + shape[axis + 1 :])
    blocks = jnp.take(blocks, order, axis=axis)
    return blocks.reshape(shape)


def per_device(student, teacher, heads):
    devices = lax.axis_size("rows")
    rows_here, model_width = student.shape
    teacher_width = teacher.shape[1]
    total_rows = rows_here * devices
    f_here = teacher_width // devices
    positions = jnp.arange(model_width)
    weights = (
        1.0
        + (positions < model_width // 4).astype(jnp.float32)
        + (positions < model_width // 2).astype(jnp.float32)
    )
    nested = jnp.minimum(weights[:, None], weights[None, :])
    gram_scale = 0.5 / total_rows

    cross_part = contract(teacher, student, 0, 0, lax.Precision.HIGH)
    moment_part = contract(student, student, 0, 0)
    d_here = model_width // devices
    partial = jnp.concatenate(
        [
            cross_part.reshape(devices, f_here, model_width),
            moment_part.reshape(devices, d_here, model_width),
        ],
        axis=1,
    ).reshape(devices * (f_here + d_here), model_width)
    reduced = lax.psum_scatter(partial, "rows", scatter_dimension=0, tiled=True)
    cross_here = reduced[:f_here]
    moment_here = reduced[f_here:]

    moment_high, moment_low = split_bf16(moment_here)
    pair = jnp.concatenate([moment_high, moment_low], axis=1)
    pair_rows = pair.size // 128
    pair = pair.reshape(pair_rows, 128)
    pair = jnp.pad(pair, ((0, f_here - pair_rows), (0, 0)))
    wide_here = jnp.concatenate([cross_here.astype(jnp.bfloat16), heads.T, pair], axis=1)
    wide_all = lax.all_gather(wide_here, "rows", axis=0, tiled=True)
    moment_all = wide_all[:, 2 * model_width :].reshape(devices, f_here, 128)[:, :pair_rows]
    moment_all = moment_all.reshape(devices, d_here, 2 * model_width)
    moment = (
        moment_all[:, :, :model_width].astype(jnp.float32)
        + moment_all[:, :, model_width:].astype(jnp.float32)
    ).reshape(model_width, model_width)
    heads_all = wide_all[:, model_width : 2 * model_width]

    grad_heads = head_scale * (
        contract(moment, heads.astype(jnp.float32), 1, 0) - cross_here.T
    )

    gram_heads = contract(heads_all, heads_all, 0, 0, lax.Precision.DEFAULT)
    teacher_high, teacher_low = split_bf16(teacher)
    teacher_wide = contract(teacher_high, wide_all, 1, 0, lax.Precision.DEFAULT) + contract(
        teacher_low, wide_all, 1, 0, lax.Precision.DEFAULT
    )
    teacher_cross = teacher_wide[:, :model_width]
    teacher_heads = teacher_wide[:, model_width : 2 * model_width]
    student_side = reg_weight * gram_heads + gram_scale * (moment * nested)
    grad_student = (
        contract(student, student_side, 1, 0)
        - reg_weight * teacher_heads
        - gram_scale * teacher_cross * weights[None, :]
    )
    return (grad_student, grad_heads)


def solution(mesh):
    in_specs = (P(("groups", "rows"), None), P(("groups", "rows"), None), P(None, "rows"))
    out_specs = (P(("groups", "rows"), None), P("groups", "rows"))
    return jax.shard_map(
        per_device, mesh=mesh, in_specs=in_specs, out_specs=out_specs, check_vma=False
    )
```

```python
import jax
import jax.numpy as jnp
from jax import lax
from jax.sharding import PartitionSpec as P

reg_weight = 0.0625
head_scale = 0.015625


def contract(left, right, left_dim, right_dim, precision=lax.Precision.HIGHEST):
    return lax.dot_general(
        left,
        right,
        (((left_dim,), (right_dim,)), ((), ())),
        precision=precision,
        preferred_element_type=jnp.float32,
    )


def split_bf16(x):
    high = lax.reduce_precision(x, exponent_bits=8, mantissa_bits=7)
    low = (x - high).astype(jnp.bfloat16)
    return high.astype(jnp.bfloat16), low


def bit_reverse_table(n):
    bits = n.bit_length() - 1
    return [int(format(j, "0%db" % bits)[::-1], 2) if bits else 0 for j in range(n)]


def gather_by_doubling(block, axis_name, axis):
    n = lax.axis_size(axis_name)
    me = lax.axis_index(axis_name)
    held = block
    bit = n.bit_length() - 2
    while bit >= 0:
        step = 1 << bit
        pairs = [(i, i ^ step) for i in range(n)]
        held = jnp.concatenate([held, lax.ppermute(held, axis_name, pairs)], axis=axis)
        bit -= 1
    rev = jnp.array(bit_reverse_table(n), jnp.int32)
    order = rev[me] ^ rev
    shape = held.shape
    blocks = held.reshape(shape[:axis] + (n, shape[axis] // n) + shape[axis + 1 :])
    blocks = jnp.take(blocks, order, axis=axis)
    return blocks.reshape(shape)


def per_device(student, teacher, heads):
    devices = lax.axis_size("rows")
    rows_here, model_width = student.shape
    teacher_width = teacher.shape[1]
    total_rows = rows_here * devices
    f_here = teacher_width // devices
    positions = jnp.arange(model_width)
    weights = (
        1.0
        + (positions < model_width // 4).astype(jnp.float32)
        + (positions < model_width // 2).astype(jnp.float32)
    )
    nested = jnp.minimum(weights[:, None], weights[None, :])
    gram_scale = 0.5 / total_rows

    cross_part = contract(teacher, student, 0, 0, lax.Precision.HIGH)
    moment_part = contract(student, student, 0, 0)
    d_here = model_width // devices
    partial = jnp.concatenate(
        [
            cross_part.reshape(devices, f_here, model_width),
            moment_part.reshape(devices, d_here, model_width),
        ],
        axis=1,
    ).reshape(devices * (f_here + d_here), model_width)
    reduced = lax.psum_scatter(partial, "rows", scatter_dimension=0, tiled=True)
    cross_here = reduced[:f_here]
    moment_here = reduced[f_here:]

    moment_high, moment_low = split_bf16(moment_here)
    pair = jnp.concatenate([moment_high, moment_low], axis=1)
    pair_rows = pair.size // 128
    pair = pair.reshape(pair_rows, 128)
    pair = jnp.pad(pair, ((0, f_here - pair_rows), (0, 0)))
    wide_here = jnp.concatenate([cross_here.astype(jnp.bfloat16), heads.T, pair], axis=1)
    wide_all = lax.all_gather(wide_here, "rows", axis=0, tiled=True)
    moment_all = wide_all[:, 2 * model_width :].reshape(devices, f_here, 128)[:, :pair_rows]
    moment_all = moment_all.reshape(devices, d_here, 2 * model_width)
    moment = (
        moment_all[:, :, :model_width].astype(jnp.float32)
        + moment_all[:, :, model_width:].astype(jnp.float32)
    ).reshape(model_width, model_width)
    heads_all = wide_all[:, model_width : 2 * model_width]

    grad_heads = head_scale * (
        contract(moment, heads.astype(jnp.float32), 1, 0) - cross_here.T
    )

    gram_heads = contract(heads_all, heads_all, 0, 0, lax.Precision.DEFAULT)
    teacher_high, teacher_low = split_bf16(teacher)
    teacher_wide = contract(
        jnp.concatenate([teacher_high, teacher_low], axis=0), wide_all, 1, 0, lax.Precision.DEFAULT
    )
    teacher_wide = teacher_wide[:rows_here] + teacher_wide[rows_here:]
    teacher_cross = teacher_wide[:, :model_width]
    teacher_heads = teacher_wide[:, model_width : 2 * model_width]
    student_side = reg_weight * gram_heads + gram_scale * (moment * nested)
    grad_student = (
        contract(student, student_side, 1, 0, lax.Precision.HIGH)
        - reg_weight * teacher_heads
        - gram_scale * teacher_cross * weights[None, :]
    )
    return (grad_student, grad_heads)


def solution(mesh):
    in_specs = (P(("groups", "rows"), None), P(("groups", "rows"), None), P(None, "rows"))
    out_specs = (P(("groups", "rows"), None), P("groups", "rows"))
    return jax.shard_map(
        per_device, mesh=mesh, in_specs=in_specs, out_specs=out_specs, check_vma=False
    )
```

```python
import jax
import jax.numpy as jnp
from jax import lax
from jax.sharding import PartitionSpec as P

reg_weight = 0.0625
head_scale = 0.015625


def contract(left, right, left_dim, right_dim, precision=lax.Precision.HIGHEST):
    return lax.dot_general(
        left,
        right,
        (((left_dim,), (right_dim,)), ((), ())),
        precision=precision,
        preferred_element_type=jnp.float32,
    )


def split_bf16(x):
    high = lax.reduce_precision(x, exponent_bits=8, mantissa_bits=7)
    low = (x - high).astype(jnp.bfloat16)
    return high.astype(jnp.bfloat16), low


def bit_reverse_table(n):
    bits = n.bit_length() - 1
    return [int(format(j, "0%db" % bits)[::-1], 2) if bits else 0 for j in range(n)]


def gather_by_doubling(block, axis_name, axis):
    n = lax.axis_size(axis_name)
    me = lax.axis_index(axis_name)
    held = block
    bit = n.bit_length() - 2
    while bit >= 0:
        step = 1 << bit
        pairs = [(i, i ^ step) for i in range(n)]
        held = jnp.concatenate([held, lax.ppermute(held, axis_name, pairs)], axis=axis)
        bit -= 1
    rev = jnp.array(bit_reverse_table(n), jnp.int32)
    order = rev[me] ^ rev
    shape = held.shape
    blocks = held.reshape(shape[:axis] + (n, shape[axis] // n) + shape[axis + 1 :])
    blocks = jnp.take(blocks, order, axis=axis)
    return blocks.reshape(shape)


def per_device(student, teacher, heads):
    devices = lax.axis_size("rows")
    rows_here, model_width = student.shape
    teacher_width = teacher.shape[1]
    total_rows = rows_here * devices
    f_here = teacher_width // devices
    positions = jnp.arange(model_width)
    weights = (
        1.0
        + (positions < model_width // 4).astype(jnp.float32)
        + (positions < model_width // 2).astype(jnp.float32)
    )
    nested = jnp.minimum(weights[:, None], weights[None, :])
    gram_scale = 0.5 / total_rows

    group = lax.axis_index("groups")
    half = heads.shape[1] // 2
    mine = lax.dynamic_slice_in_dim(heads, group * half, half, axis=1)
    heads_parts = lax.all_gather(mine, ("groups", "rows"), axis=0, tiled=False)

    cross_part = contract(teacher, student, 0, 0, lax.Precision.HIGH)
    moment_part = contract(student, student, 0, 0)
    d_here = model_width // devices
    partial = jnp.concatenate(
        [
            cross_part.reshape(devices, f_here, model_width),
            moment_part.reshape(devices, d_here, model_width),
        ],
        axis=1,
    ).reshape(devices * (f_here + d_here), model_width)
    heads_parts, partial = lax.optimization_barrier((heads_parts, partial))
    heads_all = heads_parts.reshape(2, devices, model_width, half).transpose(2, 1, 0, 3)
    heads_all = heads_all.reshape(model_width, teacher_width)
    reduced = lax.psum_scatter(partial, "rows", scatter_dimension=0, tiled=True)
    cross_here = reduced[:f_here]
    moment_here = reduced[f_here:]

    moment_high, moment_low = split_bf16(moment_here)
    pair = jnp.concatenate([moment_high, moment_low], axis=1)
    pair_rows = pair.size // 128
    pair = pair.reshape(pair_rows, 128)
    pair = jnp.pad(pair, ((0, f_here - pair_rows), (0, 0)))
    wide_here = jnp.concatenate([cross_here.astype(jnp.bfloat16), pair], axis=1)
    wide_all = lax.all_gather(wide_here, "rows", axis=0, tiled=True)
    moment_all = wide_all[:, model_width:].reshape(devices, f_here, 128)[:, :pair_rows]
    moment_all = moment_all.reshape(devices, d_here, 2 * model_width)
    moment = (
        moment_all[:, :, :model_width].astype(jnp.float32)
        + moment_all[:, :, model_width:].astype(jnp.float32)
    ).reshape(model_width, model_width)

    grad_heads = head_scale * (
        contract(moment, heads.astype(jnp.float32), 1, 0) - cross_here.T
    )

    gram_heads = contract(heads_all, heads_all, 1, 1, lax.Precision.DEFAULT)
    teacher_high, teacher_low = split_bf16(teacher)
    teacher_pair = jnp.concatenate([teacher_high, teacher_low], axis=0)
    teacher_heads = contract(teacher_pair, heads_all, 1, 1, lax.Precision.DEFAULT)
    teacher_heads = teacher_heads[:rows_here] + teacher_heads[rows_here:]
    teacher_cross = contract(teacher_pair, wide_all, 1, 0, lax.Precision.DEFAULT)
    teacher_cross = (teacher_cross[:rows_here] + teacher_cross[rows_here:])[:, :model_width]
    student_side = reg_weight * gram_heads + gram_scale * (moment * nested)
    grad_student = (
        contract(student, student_side, 1, 0, lax.Precision.HIGH)
        - reg_weight * teacher_heads
        - gram_scale * teacher_cross * weights[None, :]
    )
    return (grad_student, grad_heads)


def solution(mesh):
    in_specs = (P(("groups", "rows"), None), P(("groups", "rows"), None), P(None, "rows"))
    out_specs = (P(("groups", "rows"), None), P("groups", "rows"))
    return jax.shard_map(
        per_device, mesh=mesh, in_specs=in_specs, out_specs=out_specs, check_vma=False
    )
```

```python
import jax
import jax.numpy as jnp
from jax import lax
from jax.sharding import PartitionSpec as P

reg_weight = 0.0625
head_scale = 0.015625


def contract(left, right, left_dim, right_dim, precision=lax.Precision.HIGHEST):
    return lax.dot_general(
        left,
        right,
        (((left_dim,), (right_dim,)), ((), ())),
        precision=precision,
        preferred_element_type=jnp.float32,
    )


def split_bf16(x):
    high = lax.reduce_precision(x, exponent_bits=8, mantissa_bits=7)
    low = (x - high).astype(jnp.bfloat16)
    return high.astype(jnp.bfloat16), low


def per_device(student, teacher, heads):
    devices = lax.axis_size("rows")
    rows_here, model_width = student.shape
    teacher_width = teacher.shape[1]
    total_rows = rows_here * devices
    f_here = teacher_width // devices
    d_here = model_width // devices
    positions = jnp.arange(model_width)
    weights = (
        1.0
        + (positions < model_width // 4).astype(jnp.float32)
        + (positions < model_width // 2).astype(jnp.float32)
    )
    nested = jnp.minimum(weights[:, None], weights[None, :])
    gram_scale = 0.5 / total_rows

    heads_all = lax.all_gather(heads, "rows", axis=1, tiled=True)

    left = jnp.concatenate(
        [
            teacher.reshape(rows_here, devices, f_here),
            student.reshape(rows_here, devices, d_here),
        ],
        axis=2,
    ).reshape(rows_here, devices * (f_here + d_here))
    partial = contract(left, student, 0, 0, lax.Precision.HIGH)
    heads_all, partial = lax.optimization_barrier((heads_all, partial))
    reduced = lax.psum_scatter(partial, "rows", scatter_dimension=0, tiled=True)
    cross_here = reduced[:f_here]
    moment_here = reduced[f_here:]

    moment_high, moment_low = split_bf16(moment_here)
    packed = jnp.concatenate(
        [cross_here.astype(jnp.bfloat16), moment_high, moment_low], axis=0
    )
    gathered = lax.all_gather(packed, "rows", axis=0, tiled=False)
    cross_low = gathered[:, :f_here].reshape(teacher_width, model_width)
    moment = (
        gathered[:, f_here : f_here + d_here].astype(jnp.float32)
        + gathered[:, f_here + d_here :].astype(jnp.float32)
    ).reshape(model_width, model_width)

    grad_heads = head_scale * (
        contract(moment, heads.astype(jnp.float32), 1, 0, lax.Precision.HIGH) - cross_here.T
    )

    gram_heads = contract(heads_all, heads_all, 1, 1, lax.Precision.DEFAULT)
    teacher_high, teacher_low = split_bf16(teacher)
    teacher_pair = jnp.concatenate([teacher_high, teacher_low], axis=0)
    teacher_heads = contract(teacher_pair, heads_all, 1, 1, lax.Precision.DEFAULT)
    teacher_heads = teacher_heads[:rows_here] + teacher_heads[rows_here:]
    teacher_cross = contract(teacher_pair, cross_low, 1, 0, lax.Precision.DEFAULT)
    teacher_cross = teacher_cross[:rows_here] + teacher_cross[rows_here:]
    student_side = reg_weight * gram_heads + gram_scale * (moment * nested)
    grad_student = (
        contract(student, student_side, 1, 0, lax.Precision.HIGH)
        - reg_weight * teacher_heads
        - gram_scale * teacher_cross * weights[None, :]
    )
    return (grad_student, grad_heads)


def solution(mesh):
    in_specs = (P(("groups", "rows"), None), P(("groups", "rows"), None), P(None, "rows"))
    out_specs = (P(("groups", "rows"), None), P("groups", "rows"))
    return jax.shard_map(
        per_device, mesh=mesh, in_specs=in_specs, out_specs=out_specs, check_vma=False
    )
```

```python
import jax
import jax.numpy as jnp
from jax import lax
from jax.sharding import PartitionSpec as P

reg_weight = 0.0625
head_scale = 0.015625


def contract(left, right, left_dim, right_dim, precision=lax.Precision.HIGHEST):
    return lax.dot_general(
        left,
        right,
        (((left_dim,), (right_dim,)), ((), ())),
        precision=precision,
        preferred_element_type=jnp.float32,
    )


def split_bf16(x):
    high = lax.reduce_precision(x, exponent_bits=8, mantissa_bits=7)
    low = (x - high).astype(jnp.bfloat16)
    return high.astype(jnp.bfloat16), low


def per_device(student, teacher, heads):
    devices = lax.axis_size("rows")
    rows_here, model_width = student.shape
    teacher_width = teacher.shape[1]
    total_rows = rows_here * devices
    f_here = teacher_width // devices
    d_here = model_width // devices
    positions = jnp.arange(model_width)
    weights = (
        1.0
        + (positions < model_width // 4).astype(jnp.float32)
        + (positions < model_width // 2).astype(jnp.float32)
    )
    nested = jnp.minimum(weights[:, None], weights[None, :])
    gram_scale = 0.5 / total_rows

    heads_all = lax.all_gather(heads, "rows", axis=1, tiled=True)

    left = jnp.concatenate(
        [
            teacher.reshape(rows_here, devices, f_here),
            student.reshape(rows_here, devices, d_here),
        ],
        axis=2,
    ).reshape(rows_here, devices * (f_here + d_here))
    partial = contract(left, student, 0, 0, lax.Precision.HIGH)
    heads_all, partial = lax.optimization_barrier((heads_all, partial))
    reduced = lax.psum_scatter(partial, "rows", scatter_dimension=0, tiled=True)
    cross_here = reduced[:f_here]
    moment_here = reduced[f_here:]

    moment_high, moment_low = split_bf16(moment_here)
    packed = jnp.concatenate(
        [cross_here.astype(jnp.bfloat16), moment_high, moment_low], axis=0
    )
    gram_heads = contract(heads_all, heads_all, 1, 1, lax.Precision.DEFAULT)
    teacher_high, teacher_low = split_bf16(teacher)
    teacher_pair = jnp.concatenate([teacher_high, teacher_low], axis=0)
    teacher_heads = contract(teacher_pair, heads_all, 1, 1, lax.Precision.DEFAULT)
    teacher_heads = teacher_heads[:rows_here] + teacher_heads[rows_here:]
    gram_heads, teacher_heads, packed = lax.optimization_barrier(
        (gram_heads, teacher_heads, packed)
    )
    gathered = lax.all_gather(packed, "rows", axis=0, tiled=False)
    cross_low = gathered[:, :f_here].reshape(teacher_width, model_width)
    moment = (
        gathered[:, f_here : f_here + d_here].astype(jnp.float32)
        + gathered[:, f_here + d_here :].astype(jnp.float32)
    ).reshape(model_width, model_width)

    grad_heads = head_scale * (
        contract(moment, heads.astype(jnp.float32), 1, 0, lax.Precision.HIGH) - cross_here.T
    )

    teacher_cross = contract(teacher_pair, cross_low, 1, 0, lax.Precision.DEFAULT)
    teacher_cross = teacher_cross[:rows_here] + teacher_cross[rows_here:]
    student_side = reg_weight * gram_heads + gram_scale * (moment * nested)
    grad_student = (
        contract(student, student_side, 1, 0, lax.Precision.HIGH)
        - reg_weight * teacher_heads
        - gram_scale * teacher_cross * weights[None, :]
    )
    return (grad_student, grad_heads)


def solution(mesh):
    in_specs = (P(("groups", "rows"), None), P(("groups", "rows"), None), P(None, "rows"))
    out_specs = (P(("groups", "rows"), None), P("groups", "rows"))
    return jax.shard_map(
        per_device, mesh=mesh, in_specs=in_specs, out_specs=out_specs, check_vma=False
    )
```

```python
import jax
import jax.numpy as jnp
from jax import lax
from jax.sharding import PartitionSpec as P

reg_weight = 0.0625
head_scale = 0.015625


def contract(left, right, left_dim, right_dim, precision=lax.Precision.HIGHEST):
    return lax.dot_general(
        left,
        right,
        (((left_dim,), (right_dim,)), ((), ())),
        precision=precision,
        preferred_element_type=jnp.float32,
    )


def split_bf16(x):
    high = lax.reduce_precision(x, exponent_bits=8, mantissa_bits=7)
    low = (x - high).astype(jnp.bfloat16)
    return high.astype(jnp.bfloat16), low


def per_device(student, teacher, heads):
    devices = lax.axis_size("rows")
    rows_here, model_width = student.shape
    teacher_width = teacher.shape[1]
    total_rows = rows_here * devices
    f_here = teacher_width // devices
    d_here = model_width // devices
    positions = jnp.arange(model_width)
    weights = (
        1.0
        + (positions < model_width // 4).astype(jnp.float32)
        + (positions < model_width // 2).astype(jnp.float32)
    )
    nested = jnp.minimum(weights[:, None], weights[None, :])
    gram_scale = 0.5 / total_rows

    group = lax.axis_index("groups")
    half = heads.shape[1] // 2
    mine = lax.dynamic_slice_in_dim(heads, group * half, half, axis=1)
    mine = lax.all_gather(mine, "rows", axis=0, tiled=False)

    left = jnp.concatenate(
        [
            teacher.reshape(rows_here, devices, f_here),
            student.reshape(rows_here, devices, d_here),
        ],
        axis=2,
    ).reshape(rows_here, devices * (f_here + d_here))
    partial = contract(left, student, 0, 0, lax.Precision.HIGH)
    mine, partial = lax.optimization_barrier((mine, partial))
    theirs = lax.ppermute(mine, "groups", [(0, 1), (1, 0)])
    first = group == 0
    heads_all = jnp.stack(
        [jnp.where(first, mine, theirs), jnp.where(first, theirs, mine)], axis=1
    )
    heads_all = heads_all.transpose(2, 0, 1, 3).reshape(model_width, teacher_width)
    reduced = lax.psum_scatter(partial, "rows", scatter_dimension=0, tiled=True)
    cross_here = reduced[:f_here]
    moment_here = reduced[f_here:]

    moment_high, moment_low = split_bf16(moment_here)
    packed = jnp.concatenate(
        [cross_here.astype(jnp.bfloat16), moment_high, moment_low], axis=0
    )
    gram_heads = contract(heads_all, heads_all, 1, 1, lax.Precision.DEFAULT)
    teacher_high, teacher_low = split_bf16(teacher)
    teacher_pair = jnp.concatenate([teacher_high, teacher_low], axis=0)
    teacher_heads = contract(teacher_pair, heads_all, 1, 1, lax.Precision.DEFAULT)
    teacher_heads = teacher_heads[:rows_here] + teacher_heads[rows_here:]
    gram_heads, teacher_heads, packed = lax.optimization_barrier(
        (gram_heads, teacher_heads, packed)
    )
    gathered = lax.all_gather(packed, "rows", axis=0, tiled=False)
    cross_low = gathered[:, :f_here].reshape(teacher_width, model_width)
    moment = (
        gathered[:, f_here : f_here + d_here].astype(jnp.float32)
        + gathered[:, f_here + d_here :].astype(jnp.float32)
    ).reshape(model_width, model_width)

    grad_heads = head_scale * (
        contract(moment, heads.astype(jnp.float32), 1, 0, lax.Precision.HIGH) - cross_here.T
    )

    teacher_cross = contract(teacher_pair, cross_low, 1, 0, lax.Precision.DEFAULT)
    teacher_cross = teacher_cross[:rows_here] + teacher_cross[rows_here:]
    student_side = reg_weight * gram_heads + gram_scale * (moment * nested)
    grad_student = (
        contract(student, student_side, 1, 0, lax.Precision.HIGH)
        - reg_weight * teacher_heads
        - gram_scale * teacher_cross * weights[None, :]
    )
    return (grad_student, grad_heads)


def solution(mesh):
    in_specs = (P(("groups", "rows"), None), P(("groups", "rows"), None), P(None, "rows"))
    out_specs = (P(("groups", "rows"), None), P("groups", "rows"))
    return jax.shard_map(
        per_device, mesh=mesh, in_specs=in_specs, out_specs=out_specs, check_vma=False
    )
```

```python
import jax
import jax.numpy as jnp
from jax import lax
from jax.sharding import PartitionSpec as P

reg_weight = 0.0625
head_scale = 0.015625


def contract(left, right, left_dim, right_dim, precision=lax.Precision.HIGHEST):
    return lax.dot_general(
        left,
        right,
        (((left_dim,), (right_dim,)), ((), ())),
        precision=precision,
        preferred_element_type=jnp.float32,
    )


def split_bf16(x):
    high = lax.reduce_precision(x, exponent_bits=8, mantissa_bits=7)
    low = (x - high).astype(jnp.bfloat16)
    return high.astype(jnp.bfloat16), low


def per_device(student, teacher, heads):
    devices = lax.axis_size("rows")
    rows_here, model_width = student.shape
    teacher_width = teacher.shape[1]
    total_rows = rows_here * devices
    f_here = teacher_width // devices
    d_here = model_width // devices
    positions = jnp.arange(model_width)
    weights = (
        1.0
        + (positions < model_width // 4).astype(jnp.float32)
        + (positions < model_width // 2).astype(jnp.float32)
    )
    nested = jnp.minimum(weights[:, None], weights[None, :])
    gram_scale = 0.5 / total_rows

    group = lax.axis_index("groups")
    half = f_here // 2
    mine = lax.dynamic_slice_in_dim(heads.T, group * half, half, axis=0)
    mine = lax.all_gather(mine, "rows", axis=0, tiled=False)

    left = jnp.concatenate(
        [
            teacher.reshape(rows_here, devices, f_here),
            student.reshape(rows_here, devices, d_here),
        ],
        axis=2,
    ).reshape(rows_here, devices * (f_here + d_here))
    partial = contract(left, student, 0, 0, lax.Precision.HIGH)
    mine, partial = lax.optimization_barrier((mine, partial))
    theirs = lax.ppermute(mine, "groups", [(0, 1), (1, 0)])
    first = group == 0
    d_here = model_width // devices
    heads_all = jnp.concatenate(
        [
            jnp.where(first, mine, theirs),
            jnp.where(first, theirs, mine),
            jnp.zeros((devices, 2 * d_here, model_width), mine.dtype),
        ],
        axis=1,
    ).reshape(devices * (f_here + 2 * d_here), model_width)
    reduced = lax.psum_scatter(partial, "rows", scatter_dimension=0, tiled=True)
    cross_here = reduced[:f_here]
    moment_here = reduced[f_here:]

    moment_high, moment_low = split_bf16(moment_here)
    packed = jnp.concatenate(
        [cross_here.astype(jnp.bfloat16), moment_high, moment_low], axis=0
    )
    gram_heads = contract(heads_all, heads_all, 0, 0, lax.Precision.DEFAULT)
    teacher_high, teacher_low = split_bf16(teacher)
    teacher_pair = jnp.concatenate([teacher_high, teacher_low], axis=0)
    teacher_pair = jnp.pad(
        teacher_pair.reshape(2 * rows_here, devices, f_here), ((0, 0), (0, 0), (0, 2 * d_here))
    ).reshape(2 * rows_here, devices * (f_here + 2 * d_here))
    teacher_heads = contract(teacher_pair, heads_all, 1, 0, lax.Precision.DEFAULT)
    teacher_heads = teacher_heads[:rows_here] + teacher_heads[rows_here:]
    gram_heads, teacher_heads, packed = lax.optimization_barrier(
        (gram_heads, teacher_heads, packed)
    )
    gathered = lax.all_gather(packed, "rows", axis=0, tiled=False)
    moment = (
        gathered[:, f_here : f_here + d_here].astype(jnp.float32)
        + gathered[:, f_here + d_here :].astype(jnp.float32)
    ).reshape(model_width, model_width)

    grad_heads = head_scale * (
        contract(moment, heads.astype(jnp.float32), 1, 0, lax.Precision.HIGH) - cross_here.T
    )

    teacher_cross = contract(
        teacher_pair, gathered.reshape(-1, model_width), 1, 0, lax.Precision.DEFAULT
    )
    teacher_cross = teacher_cross[:rows_here] + teacher_cross[rows_here:]
    student_side = reg_weight * gram_heads + gram_scale * (moment * nested)
    grad_student = (
        contract(student, student_side, 1, 0, lax.Precision.HIGH)
        - reg_weight * teacher_heads
        - gram_scale * teacher_cross * weights[None, :]
    )
    return (grad_student, grad_heads)


def solution(mesh):
    in_specs = (P(("groups", "rows"), None), P(("groups", "rows"), None), P(None, "rows"))
    out_specs = (P(("groups", "rows"), None), P("groups", "rows"))
    return jax.shard_map(
        per_device, mesh=mesh, in_specs=in_specs, out_specs=out_specs, check_vma=False
    )
```

```python
import jax
import jax.numpy as jnp
from jax import lax
from jax.sharding import PartitionSpec as P

reg_weight = 0.0625
head_scale = 0.015625


def contract(left, right, left_dim, right_dim, precision=lax.Precision.HIGHEST):
    return lax.dot_general(
        left,
        right,
        (((left_dim,), (right_dim,)), ((), ())),
        precision=precision,
        preferred_element_type=jnp.float32,
    )


def split_bf16(x):
    high = lax.reduce_precision(x, exponent_bits=8, mantissa_bits=7)
    low = (x - high).astype(jnp.bfloat16)
    return high.astype(jnp.bfloat16), low


def per_device(student, teacher, heads):
    devices = lax.axis_size("rows")
    rows_here, model_width = student.shape
    teacher_width = teacher.shape[1]
    total_rows = rows_here * devices
    f_here = teacher_width // devices
    d_here = model_width // devices
    positions = jnp.arange(model_width)
    weights = (
        1.0
        + (positions < model_width // 4).astype(jnp.float32)
        + (positions < model_width // 2).astype(jnp.float32)
    )
    nested = jnp.minimum(weights[:, None], weights[None, :])
    gram_scale = 0.5 / total_rows

    group = lax.axis_index("groups")
    half = f_here // 2
    mine = lax.dynamic_slice_in_dim(heads.T, group * half, half, axis=0)
    mine = lax.all_gather(mine, "rows", axis=0, tiled=False)

    left = jnp.concatenate(
        [
            teacher.reshape(rows_here, devices, f_here),
            student.reshape(rows_here, devices, d_here),
        ],
        axis=2,
    ).reshape(rows_here, devices * (f_here + d_here))
    partial = contract(left, student, 0, 0, lax.Precision.HIGH)
    mine, partial = lax.optimization_barrier((mine, partial))
    theirs = lax.ppermute(mine, "groups", [(0, 1), (1, 0)])
    first = group == 0
    heads_all = jnp.concatenate(
        [jnp.where(first, mine, theirs), jnp.where(first, theirs, mine)], axis=1
    ).reshape(teacher_width, model_width)
    reduced = lax.psum_scatter(partial, "rows", scatter_dimension=0, tiled=True)
    cross_here = reduced[:f_here]
    moment_here = reduced[f_here:]

    moment_high, moment_low = split_bf16(moment_here)
    packed = jnp.concatenate(
        [cross_here.astype(jnp.bfloat16), moment_high, moment_low], axis=0
    )
    gram_heads = contract(heads_all, heads_all, 0, 0, lax.Precision.DEFAULT)
    teacher_high, teacher_low = split_bf16(teacher)
    teacher_pair = jnp.concatenate([teacher_high, teacher_low], axis=0)
    teacher_heads = contract(teacher_pair, heads_all, 1, 0, lax.Precision.DEFAULT)
    teacher_heads = teacher_heads[:rows_here] + teacher_heads[rows_here:]
    gram_heads, teacher_heads, packed = lax.optimization_barrier(
        (gram_heads, teacher_heads, packed)
    )
    gathered = lax.all_gather(packed, "rows", axis=0, tiled=False)
    moment = (
        gathered[:, f_here : f_here + d_here].astype(jnp.float32)
        + gathered[:, f_here + d_here :].astype(jnp.float32)
    ).reshape(model_width, model_width)

    grad_heads = head_scale * (
        contract(moment, heads.astype(jnp.float32), 1, 0, lax.Precision.HIGH) - cross_here.T
    )

    cross_low = gathered[:, :f_here].reshape(teacher_width, model_width)
    teacher_cross = contract(teacher_pair, cross_low, 1, 0, lax.Precision.DEFAULT)
    teacher_cross = teacher_cross[:rows_here] + teacher_cross[rows_here:]
    student_side = reg_weight * gram_heads + gram_scale * (moment * nested)
    grad_student = (
        contract(student, student_side, 1, 0, lax.Precision.HIGH)
        - reg_weight * teacher_heads
        - gram_scale * teacher_cross * weights[None, :]
    )
    return (grad_student, grad_heads)


def solution(mesh):
    in_specs = (P(("groups", "rows"), None), P(("groups", "rows"), None), P(None, "rows"))
    out_specs = (P(("groups", "rows"), None), P("groups", "rows"))
    return jax.shard_map(
        per_device, mesh=mesh, in_specs=in_specs, out_specs=out_specs, check_vma=False
    )
```

```python
import jax
import jax.numpy as jnp
from jax import lax
from jax.sharding import PartitionSpec as P

reg_weight = 0.0625
head_scale = 0.015625


def contract(left, right, left_dim, right_dim, precision=lax.Precision.HIGHEST):
    return lax.dot_general(
        left,
        right,
        (((left_dim,), (right_dim,)), ((), ())),
        precision=precision,
        preferred_element_type=jnp.float32,
    )


def split_bf16(x):
    high = lax.reduce_precision(x, exponent_bits=8, mantissa_bits=7)
    low = (x - high).astype(jnp.bfloat16)
    return high.astype(jnp.bfloat16), low


def per_device(student, teacher, heads):
    devices = lax.axis_size("rows")
    rows_here, model_width = student.shape
    teacher_width = teacher.shape[1]
    total_rows = rows_here * devices
    f_here = teacher_width // devices
    d_here = model_width // devices
    positions = jnp.arange(model_width)
    weights = (
        1.0
        + (positions < model_width // 4).astype(jnp.float32)
        + (positions < model_width // 2).astype(jnp.float32)
    )
    nested = jnp.minimum(weights[:, None], weights[None, :])
    gram_scale = 0.5 / total_rows

    group = lax.axis_index("groups")
    half = f_here // 2
    mine = lax.dynamic_slice_in_dim(heads.T, group * half, half, axis=0)
    mine = lax.all_gather(mine, "rows", axis=0, tiled=False)

    left = jnp.concatenate(
        [
            teacher.reshape(rows_here, devices, f_here),
            student.reshape(rows_here, devices, d_here),
        ],
        axis=2,
    ).reshape(rows_here, devices * (f_here + d_here))
    partial = contract(left, student, 0, 0, lax.Precision.HIGH)
    mine, partial = lax.optimization_barrier((mine, partial))
    theirs = lax.ppermute(mine, "groups", [(0, 1), (1, 0)])
    first = group == 0
    heads_all = jnp.concatenate(
        [jnp.where(first, mine, theirs), jnp.where(first, theirs, mine)], axis=1
    ).reshape(teacher_width, model_width)
    reduced = lax.psum_scatter(partial, "rows", scatter_dimension=0, tiled=True)
    cross_here = reduced[:f_here]
    moment_here = reduced[f_here:]

    moment_high, moment_low = split_bf16(moment_here)
    packed = jnp.concatenate(
        [cross_here.astype(jnp.bfloat16), moment_high, moment_low], axis=0
    )
    gram_heads = contract(heads_all, heads_all, 0, 0, lax.Precision.DEFAULT)
    teacher_high, teacher_low = split_bf16(teacher)
    teacher_pair = jnp.concatenate([teacher_high, teacher_low], axis=0)
    teacher_heads = contract(teacher_pair, heads_all, 1, 0, lax.Precision.DEFAULT)
    teacher_heads = teacher_heads[:rows_here] + teacher_heads[rows_here:]
    gram_heads, teacher_heads, packed = lax.optimization_barrier(
        (gram_heads, teacher_heads, packed)
    )
    gathered = lax.all_gather(packed, "rows", axis=0, tiled=False)
    moment = (
        gathered[:, f_here : f_here + d_here].astype(jnp.float32)
        + gathered[:, f_here + d_here :].astype(jnp.float32)
    ).reshape(model_width, model_width)

    grad_heads = head_scale * (
        contract(moment, heads.astype(jnp.float32), 1, 0, lax.Precision.HIGH) - cross_here.T
    )

    teacher_cross = lax.dot_general(
        teacher_pair.reshape(2 * rows_here, devices, f_here),
        gathered[:, :f_here],
        (((1, 2), (0, 1)), ((), ())),
        preferred_element_type=jnp.float32,
    )
    teacher_cross = teacher_cross[:rows_here] + teacher_cross[rows_here:]
    student_side = reg_weight * gram_heads + gram_scale * (moment * nested)
    grad_student = (
        contract(student, student_side, 1, 0, lax.Precision.HIGH)
        - reg_weight * teacher_heads
        - gram_scale * teacher_cross * weights[None, :]
    )
    return (grad_student, grad_heads)


def solution(mesh):
    in_specs = (P(("groups", "rows"), None), P(("groups", "rows"), None), P(None, "rows"))
    out_specs = (P(("groups", "rows"), None), P("groups", "rows"))
    return jax.shard_map(
        per_device, mesh=mesh, in_specs=in_specs, out_specs=out_specs, check_vma=False
    )
```

```python
import jax
import jax.numpy as jnp
from jax import lax
from jax.sharding import PartitionSpec as P

reg_weight = 0.0625
head_scale = 0.015625


def contract(left, right, left_dim, right_dim, precision=lax.Precision.HIGHEST):
    return lax.dot_general(
        left,
        right,
        (((left_dim,), (right_dim,)), ((), ())),
        precision=precision,
        preferred_element_type=jnp.float32,
    )


def split_bf16(x):
    high = lax.reduce_precision(x, exponent_bits=8, mantissa_bits=7)
    low = (x - high).astype(jnp.bfloat16)
    return high.astype(jnp.bfloat16), low


def per_device(student, teacher, heads):
    devices = lax.axis_size("rows")
    rows_here, model_width = student.shape
    teacher_width = teacher.shape[1]
    total_rows = rows_here * devices
    f_here = teacher_width // devices
    d_here = model_width // devices
    positions = jnp.arange(model_width)
    weights = (
        1.0
        + (positions < model_width // 4).astype(jnp.float32)
        + (positions < model_width // 2).astype(jnp.float32)
    )
    nested = jnp.minimum(weights[:, None], weights[None, :])
    gram_scale = 0.5 / total_rows

    group = lax.axis_index("groups")
    half = f_here // 2
    mine = lax.dynamic_slice_in_dim(heads.T, group * half, half, axis=0)
    mine = lax.all_gather(mine, "rows", axis=0, tiled=False)

    left = jnp.concatenate(
        [
            teacher.reshape(rows_here, devices, f_here),
            student.reshape(rows_here, devices, d_here),
        ],
        axis=2,
    ).reshape(rows_here, devices * (f_here + d_here))
    partial = contract(left, student, 0, 0, lax.Precision.HIGH)
    mine, partial = lax.optimization_barrier((mine, partial))
    theirs = lax.ppermute(mine, "groups", [(0, 1), (1, 0)])
    first = group == 0
    heads_all = jnp.concatenate(
        [jnp.where(first, mine, theirs), jnp.where(first, theirs, mine)], axis=1
    ).reshape(teacher_width, model_width)
    reduced = lax.psum_scatter(partial, "rows", scatter_dimension=0, tiled=True)
    cross_here = reduced[:f_here]
    moment_here = reduced[f_here:]

    moment_high, moment_low = split_bf16(moment_here)
    packed = jnp.concatenate(
        [cross_here.astype(jnp.bfloat16), moment_high, moment_low], axis=0
    )
    gram_heads = contract(heads_all, heads_all, 0, 0, lax.Precision.DEFAULT)
    teacher_high, teacher_low = split_bf16(teacher)
    teacher_pair = jnp.concatenate([teacher_high, teacher_low], axis=0)
    teacher_heads = contract(teacher_pair, heads_all, 1, 0, lax.Precision.DEFAULT)
    teacher_heads = teacher_heads[:rows_here] + teacher_heads[rows_here:]
    heads_terms = reg_weight * (
        contract(student, gram_heads, 1, 0, lax.Precision.HIGH) - teacher_heads
    )
    heads_terms, packed = lax.optimization_barrier((heads_terms, packed))
    gathered = lax.all_gather(packed, "rows", axis=0, tiled=False)
    moment = (
        gathered[:, f_here : f_here + d_here].astype(jnp.float32)
        + gathered[:, f_here + d_here :].astype(jnp.float32)
    ).reshape(model_width, model_width)

    grad_heads = head_scale * (
        contract(moment, heads.astype(jnp.float32), 1, 0, lax.Precision.HIGH) - cross_here.T
    )

    teacher_cross = lax.dot_general(
        teacher_pair.reshape(2 * rows_here, devices, f_here),
        gathered[:, :f_here],
        (((1, 2), (0, 1)), ((), ())),
        preferred_element_type=jnp.float32,
    )
    teacher_cross = teacher_cross[:rows_here] + teacher_cross[rows_here:]
    grad_student = heads_terms + gram_scale * (
        contract(student, moment * nested, 1, 0, lax.Precision.HIGH)
        - teacher_cross * weights[None, :]
    )
    return (grad_student, grad_heads)


def solution(mesh):
    in_specs = (P(("groups", "rows"), None), P(("groups", "rows"), None), P(None, "rows"))
    out_specs = (P(("groups", "rows"), None), P("groups", "rows"))
    return jax.shard_map(
        per_device, mesh=mesh, in_specs=in_specs, out_specs=out_specs, check_vma=False
    )
```

```python
import jax
import jax.numpy as jnp
from jax import lax
from jax.sharding import PartitionSpec as P

reg_weight = 0.0625
head_scale = 0.015625


def contract(left, right, left_dim, right_dim, precision=lax.Precision.HIGHEST):
    return lax.dot_general(
        left,
        right,
        (((left_dim,), (right_dim,)), ((), ())),
        precision=precision,
        preferred_element_type=jnp.float32,
    )


def split_bf16(x):
    high = lax.reduce_precision(x, exponent_bits=8, mantissa_bits=7)
    low = (x - high).astype(jnp.bfloat16)
    return high.astype(jnp.bfloat16), low


def per_device(student, teacher, heads):
    devices = lax.axis_size("rows")
    rows_here, model_width = student.shape
    teacher_width = teacher.shape[1]
    total_rows = rows_here * devices
    f_here = teacher_width // devices
    d_here = model_width // devices
    positions = jnp.arange(model_width)
    weights = (
        1.0
        + (positions < model_width // 4).astype(jnp.float32)
        + (positions < model_width // 2).astype(jnp.float32)
    )
    nested = jnp.minimum(weights[:, None], weights[None, :])
    gram_scale = 0.5 / total_rows

    group = lax.axis_index("groups")
    half = f_here // 2
    mine = lax.dynamic_slice_in_dim(heads.T, group * half, half, axis=0)
    mine = lax.all_gather(mine, "rows", axis=0, tiled=False)

    left = jnp.concatenate(
        [
            teacher.reshape(rows_here, devices, f_here),
            student.reshape(rows_here, devices, d_here),
        ],
        axis=2,
    ).reshape(rows_here, devices * (f_here + d_here))
    partial = contract(left, student, 0, 0, lax.Precision.HIGH)
    mine, partial = lax.optimization_barrier((mine, partial))
    theirs = lax.ppermute(mine, "groups", [(0, 1), (1, 0)])
    first = group == 0
    heads_all = jnp.concatenate(
        [jnp.where(first, mine, theirs), jnp.where(first, theirs, mine)], axis=1
    ).reshape(teacher_width, model_width)
    reduced = lax.psum_scatter(partial, "rows", scatter_dimension=0, tiled=True)
    cross_here = reduced[:f_here]
    moment_here = reduced[f_here:]

    moment_high, moment_low = split_bf16(moment_here)
    packed = jnp.concatenate(
        [cross_here.astype(jnp.bfloat16), moment_high, moment_low], axis=0
    )
    gram_heads = contract(heads_all, heads_all, 0, 0, lax.Precision.DEFAULT)
    teacher_high, teacher_low = split_bf16(teacher)
    teacher_pair = jnp.concatenate([teacher_high, teacher_low], axis=0)
    teacher_heads = contract(teacher_pair, heads_all, 1, 0, lax.Precision.DEFAULT)
    teacher_heads = teacher_heads[:rows_here] + teacher_heads[rows_here:]
    heads_terms = reg_weight * (
        contract(student, gram_heads, 1, 0, lax.Precision.HIGH) - teacher_heads
    )
    heads_terms, packed = lax.optimization_barrier((heads_terms, packed))
    gathered = lax.all_gather(packed, "rows", axis=0, tiled=False)
    moment_high = gathered[:, f_here : f_here + d_here].reshape(model_width, model_width)
    moment_low = gathered[:, f_here + d_here :].reshape(model_width, model_width)
    moment = moment_high.astype(jnp.float32) + moment_low.astype(jnp.float32)

    moment_heads = contract(moment_high, heads, 1, 0, lax.Precision.DEFAULT) + contract(
        moment_low, heads, 1, 0, lax.Precision.DEFAULT
    )
    grad_heads = head_scale * (moment_heads - cross_here.T)

    teacher_cross = lax.dot_general(
        teacher_pair.reshape(2 * rows_here, devices, f_here),
        gathered[:, :f_here],
        (((1, 2), (0, 1)), ((), ())),
        preferred_element_type=jnp.float32,
    )
    teacher_cross = teacher_cross[:rows_here] + teacher_cross[rows_here:]
    grad_student = heads_terms + gram_scale * (
        contract(student, moment * nested, 1, 0, lax.Precision.HIGH)
        - teacher_cross * weights[None, :]
    )
    return (grad_student, grad_heads)


def solution(mesh):
    in_specs = (P(("groups", "rows"), None), P(("groups", "rows"), None), P(None, "rows"))
    out_specs = (P(("groups", "rows"), None), P("groups", "rows"))
    return jax.shard_map(
        per_device, mesh=mesh, in_specs=in_specs, out_specs=out_specs, check_vma=False
    )
```
